256 devices in a mesh: seg: 8 (over x, core), bond: 32 (over z, y).
Axes of the slice: x: 4, y: 4, z: 8, core: 2. Of those that a mesh axis runs over, the one named last changes fastest.
Arguments:
- state: float32 [8, 32, 256, 256], P('seg', 'bond'), may hold values from -6 to 6
- left_env: bfloat16 [8, 32, 20, 256, 256], P('seg', 'bond'), as said below
- right_env: bfloat16 [8, 32, 20, 256, 256], P('seg', 'bond')
- mpo_mix: float32 [20, 20], replicated, may hold values from -1.25 to 1.25
- block_sizes: int32 [8, 32], P('seg', 'bond'), may hold values from 128 to 256
- ranks: int32 [8, 32], P('seg', 'bond'), may hold values from 64 to 128
Outputs:
- ground: float32 [8, 32, 256, 256], P('seg', 'bond')
- energy: float32 [8], P('seg')
The draws below stay inside these ranges and needn't reach their ends.
Inputs may be any that keep to these rules, and one draw needn't show every extreme that they name: Every environment matrix left_env[s,b,w] and right_env[s,b,w] is symmetric.
All inputs are finite; a program needn't handle non-finite values.
Results may differ from the reference program's by a relative error of at most 0.014.
Values may be sent and summed in bfloat16 or wider, within the bound.
No kernel may reach another device: no remote copies, remote signals or barrier semaphores. Data moves between devices by JAX's collectives and lax.ppermute only.
A program may use at most 64 MiB of HBM per device.

```python
import math
import jax
import jax.numpy as jnp
from jax import lax

BLOCK = 256
MPO = 20
LANCZOS = 4
POWER = 4
SEGS = 8
QBLOCKS = 32
N_BOND = 32


def symmetric_env(key):
    shape = (SEGS, QBLOCKS, MPO, BLOCK, BLOCK)
    base = jax.random.normal(key, shape, jnp.float32)
    sym = (base + jnp.swapaxes(base, -1, -2)) * 0.5 ** 0.5 / math.sqrt(BLOCK)
    return sym.astype(jnp.bfloat16)


def draw_left_env(key, part):
    return symmetric_env(jax.random.fold_in(key, 11))


def draw_right_env(key, part):
    return symmetric_env(jax.random.fold_in(key, 23))


def set_ends(values, stream_key, low, high):
    spot = [jax.random.randint(jax.random.fold_in(stream_key, axis), (), 0, length) for axis, length in enumerate(values.shape)]
    widest = values.shape.index(max(values.shape))
    next_to = spot[:widest] + [(spot[widest] + 1) % values.shape[widest]] + spot[widest + 1:]
    return values.at[tuple(spot)].set(low).at[tuple(next_to)].set(high)


def block_levels(key, extent, split, smallest, high):
    loudness = 1.0
    for position, parts in split:
        draws = jax.random.uniform(jax.random.fold_in(jax.random.fold_in(key, 6), position), (parts,), jnp.float32, smallest / len(split), high / len(split))
        loudness = loudness * jnp.repeat(jnp.exp(draws), extent[position] // parts).reshape((-1,) + (1,) * (len(extent) - 1 - position))
    return loudness


def scatter_about(stream_key, shape, deviation, most, pieces=(), kind=jnp.bfloat16):
    entries = jax.random.normal(stream_key, shape, jnp.float32) * deviation
    if len(pieces) > 0:
        entries = block_levels(stream_key, shape, pieces, -0.22, 0.18) * entries
    return jnp.clip(entries, min=-most, max=most).astype(kind)


def setup_inputs(seed: int = 0) -> dict:
    arg_keys = jax.random.split(jax.random.key(seed), 7)
    return {
        "state": scatter_about(arg_keys[0], (SEGS, QBLOCKS, BLOCK, BLOCK), 1.0, 6.0, ((0, 8), (1, 32)), jnp.float32),
        "left_env": draw_left_env(jax.random.fold_in(arg_keys[6], 71), 0),
        "right_env": draw_right_env(jax.random.fold_in(arg_keys[6], 71), 0),
        "mpo_mix": scatter_about(arg_keys[3], (MPO, MPO), MPO ** -0.5, 1.25, (), jnp.float32),
        "block_sizes": set_ends(jax.random.randint(arg_keys[4], (SEGS, QBLOCKS), BLOCK // 2, BLOCK + 1), jax.random.fold_in(arg_keys[4], 1), BLOCK // 2, BLOCK).astype(jnp.int32),
        "ranks": set_ends(jax.random.randint(arg_keys[5], (SEGS, QBLOCKS), BLOCK // 4, BLOCK // 2 + 1), jax.random.fold_in(arg_keys[5], 1), BLOCK // 4, (BLOCK // 2 + 1) - 1).astype(jnp.int32),
    }


def live_masks(sizes, ranks):
    index = jnp.arange(BLOCK, dtype=jnp.int32)
    live = (index[None, :] < sizes[:, None]).astype(jnp.float32)
    mask = live[:, :, None] * live[:, None, :]
    kept = (index[None, :] < ranks[:, None]).astype(jnp.float32)
    return (mask, kept)

def apply_ham(vector, left, right, mask):
    rounded = (vector * mask).astype(jnp.bfloat16)
    inner = jnp.einsum('bij,bwjk->bwik', rounded.astype(jnp.float32), right.astype(jnp.float32)).astype(jnp.bfloat16)
    outer = jnp.einsum('bwij,bwjk->bik', left.astype(jnp.float32), inner.astype(jnp.float32))
    return outer * mask

def lanczos(start, left, right, mask):
    masked = start * mask
    vector = masked / jnp.sqrt(jnp.sum(masked * masked))
    previous = jnp.zeros_like(vector)
    beta_prev = jnp.zeros((), jnp.float32)
    alphas = []
    betas = []
    basis = []
    for step in range(LANCZOS):
        image = apply_ham(vector, left, right, mask)
        alpha = jnp.sum(image * vector)
        image = image - alpha * vector - beta_prev * previous
        alphas.append(alpha)
        basis.append(vector)
        if step + 1 < LANCZOS:
            beta = jnp.sqrt(jnp.sum(image * image))
            betas.append(beta)
            previous = vector
            vector = image / beta
            beta_prev = beta
    return ritz(alphas, betas, basis)

def ritz(alphas, betas, basis):
    avec = jnp.stack(alphas)
    bvec = jnp.stack(betas)
    tri = jnp.diag(avec) + jnp.diag(bvec, 1) + jnp.diag(bvec, -1)
    zero = jnp.zeros((1,), avec.dtype)
    absb = jnp.abs(bvec)
    sigma = jnp.max(avec + jnp.concatenate([absb, zero]) + jnp.concatenate([zero, absb]))
    weights = jnp.zeros((LANCZOS,), avec.dtype).at[0].set(1.0)
    for turn in range(POWER):
        weights = sigma * weights - lax.optimization_barrier(jnp.sum(tri * weights[None, :], axis=1))
        weights = weights / jnp.sqrt(jnp.sum(weights * weights))
    result = basis[0] * weights[0]
    for step in range(1, LANCZOS):
        result = result + weights[step] * basis[step]
    energy = jnp.sum(weights * lax.optimization_barrier(jnp.sum(tri * weights[None, :], axis=1)))
    return (result, energy)

def step_one(items):
    start, left, right, mix, sizes, ranks = items
    mask, kept = live_masks(sizes, ranks)
    psi, energy = lanczos(start, left, right, mask)
    scaled = psi * math.sqrt(N_BOND * BLOCK)
    left_a = (scaled * kept[:, None, :]).astype(jnp.bfloat16).astype(jnp.float32)
    right_a = (scaled * kept[:, :, None]).astype(jnp.bfloat16).astype(jnp.float32)
    left_mix = jnp.einsum('wu,buij->bwij', mix, left.astype(jnp.float32), precision=lax.Precision.HIGHEST).astype(jnp.bfloat16)
    right_mix = jnp.einsum('wu,buij->bwij', mix, right.astype(jnp.float32), precision=lax.Precision.HIGHEST).astype(jnp.bfloat16)
    half_left = jnp.einsum('bwij,bjk->bwik', left_mix.astype(jnp.float32), left_a).astype(jnp.bfloat16)
    left_new = jnp.einsum('bji,bwjk->bwik', left_a, half_left.astype(jnp.float32)).astype(jnp.bfloat16)
    half_right = jnp.einsum('bwij,bkj->bwik', right_mix.astype(jnp.float32), right_a).astype(jnp.bfloat16)
    right_new = jnp.einsum('bij,bwjk->bwik', right_a, half_right.astype(jnp.float32)).astype(jnp.bfloat16)
    return (psi, left_new, right_new)

def step_two(items):
    start, left, right, sizes, ranks = items
    mask, kept = live_masks(sizes, ranks)
    return lanczos(start, left, right, mask)

def reference(state, left_env, right_env, mpo_mix, block_sizes, ranks):
    mixes = jnp.broadcast_to(mpo_mix, (SEGS,) + mpo_mix.shape)
    psi_one, left_new, right_new = lax.map(step_one, (state, left_env, right_env, mixes, block_sizes, ranks))
    left_in = jnp.roll(left_new, 1, axis=0)
    right_in = jnp.roll(right_new, -1, axis=0)
    psi_two, energy = lax.map(step_two, (psi_one, left_in, right_in, block_sizes, ranks))
    ground = psi_two * math.sqrt(N_BOND * BLOCK * BLOCK)
    return (ground, energy)
```

```python
import math

import jax
import jax.numpy as jnp
from jax import lax
from jax.sharding import PartitionSpec as P

LANCZOS = 4
POWER = 4


def shifted(value, axis, steps):
    count = lax.axis_size(axis)
    pairs = [(source, (source + steps) % count) for source in range(count)]
    return lax.ppermute(value, axis, pairs)


def bond_sum(value):
    count = lax.axis_size("bond")
    if count & (count - 1):
        return lax.psum(value, "bond")
    step = 1
    while step < count:
        pairs = [(source, source ^ step) for source in range(count)]
        value = value + lax.ppermute(value, "bond", pairs)
        step *= 2
    return value


def apply_ham(vector, left, right, mask):
    rounded = (vector * mask).astype(jnp.bfloat16)
    inner = jnp.einsum("ij,wjk->wik", rounded, right, preferred_element_type=jnp.float32).astype(
        jnp.bfloat16
    )
    outer = jnp.einsum("wij,wjk->ik", left, inner, preferred_element_type=jnp.float32)
    return outer * mask


def quad(first, gram, second):
    return jnp.sum(first[:, None] * gram * second[None, :])


def lanczos(start, left, right, mask):
    krylov = [start * mask]
    for step in range(LANCZOS):
        krylov.append(apply_ham(krylov[-1], left, right, mask))
    size = len(krylov)
    pairs = [(i, j) for i in range(size) for j in range(i, size)]
    local = jnp.stack([jnp.sum(krylov[i] * krylov[j]) for i, j in pairs])
    total = bond_sum(local)
    gram = jnp.zeros((size, size), jnp.float32)
    for index, (i, j) in enumerate(pairs):
        gram = gram.at[i, j].set(total[index]).at[j, i].set(total[index])

    def times_h(coef):
        return jnp.concatenate([jnp.zeros((1,), jnp.float32), coef[:-1]])

    vector = jnp.zeros((size,), jnp.float32).at[0].set(1.0) / jnp.sqrt(gram[0, 0])
    previous = jnp.zeros((size,), jnp.float32)
    beta_prev = jnp.zeros((), jnp.float32)
    alphas = []
    betas = []
    basis = []
    for step in range(LANCZOS):
        image = times_h(vector)
        alpha = quad(image, gram, vector)
        image = image - alpha * vector - beta_prev * previous
        alphas.append(alpha)
        basis.append(vector)
        if step + 1 < LANCZOS:
            beta = jnp.sqrt(quad(image, gram, image))
            betas.append(beta)
            previous = vector
            vector = image / beta
            beta_prev = beta
    avec = jnp.stack(alphas)
    bvec = jnp.stack(betas)
    tri = jnp.diag(avec) + jnp.diag(bvec, 1) + jnp.diag(bvec, -1)
    zero = jnp.zeros((1,), jnp.float32)
    absb = jnp.abs(bvec)
    sigma = jnp.max(avec + jnp.concatenate([absb, zero]) + jnp.concatenate([zero, absb]))
    weights = jnp.zeros((LANCZOS,), jnp.float32).at[0].set(1.0)
    for turn in range(POWER):
        weights = sigma * weights - jnp.sum(tri * weights[None, :], axis=1)
        weights = weights / jnp.sqrt(jnp.sum(weights * weights))
    coef = basis[0] * weights[0]
    for step in range(1, LANCZOS):
        coef = coef + weights[step] * basis[step]
    result = krylov[0] * coef[0]
    for step in range(1, LANCZOS):
        result = result + coef[step] * krylov[step]
    energy = jnp.sum(weights * jnp.sum(tri * weights[None, :], axis=1))
    return (result, energy)


def env_update(mixed, left_a):
    half_left = jnp.einsum(
        "wij,jk->wik", mixed, left_a, preferred_element_type=jnp.float32
    ).astype(jnp.bfloat16)
    return jnp.einsum(
        "ji,wjk->wik", left_a, half_left, preferred_element_type=jnp.float32
    ).astype(jnp.bfloat16)


def per_device(state, left_env, right_env, mpo_mix, block_sizes, ranks):
    blocks = lax.axis_size("bond")
    width = state.shape[-1]
    start = state[0, 0]
    left = left_env[0, 0]
    right = right_env[0, 0]
    index = jnp.arange(width, dtype=jnp.int32)
    live = (index < block_sizes[0, 0]).astype(jnp.float32)
    mask = live[:, None] * live[None, :]
    kept = (index < ranks[0, 0]).astype(jnp.float32)
    left_mix = jnp.einsum(
        "wu,uij->wij", mpo_mix, left.astype(jnp.float32), precision=lax.Precision.HIGHEST
    ).astype(jnp.bfloat16)
    right_mix = jnp.einsum(
        "wu,uij->wij", mpo_mix, right.astype(jnp.float32), precision=lax.Precision.HIGHEST
    ).astype(jnp.bfloat16)
    left_mix_got = shifted(left_mix, "seg", 1)
    right_mix_got = shifted(right_mix, "seg", -1)
    psi_one, unused = lanczos(start, left, right, mask)
    scaled = psi_one * math.sqrt(blocks * width)
    left_a = (scaled * kept[None, :]).astype(jnp.bfloat16)
    right_a = (scaled * kept[:, None]).astype(jnp.bfloat16)
    left_a_got = shifted(left_a, "seg", 1)
    right_a_got = shifted(right_a, "seg", -1)
    left_in = env_update(left_mix_got, left_a_got)
    right_in = env_update(right_mix_got, right_a_got.T)
    psi_two, energy = lanczos(psi_one, left_in, right_in, mask)
    ground = psi_two * math.sqrt(blocks * width * width)
    return (ground[None, None], jnp.reshape(energy, (1,)))


def solution(mesh):
    in_specs = (
        P("seg", "bond", None, None),
        P("seg", "bond", None, None, None),
        P("seg", "bond", None, None, None),
        P(),
        P("seg", "bond"),
        P("seg", "bond"),
    )
    out_specs = (P("seg", "bond", None, None), P("seg"))
    return jax.shard_map(
        per_device, mesh=mesh, in_specs=in_specs, out_specs=out_specs, check_vma=False
    )
```

```python
import math

import jax
import jax.numpy as jnp
from jax import lax
from jax.experimental import pallas as pl
from jax.experimental.pallas import tpu as pltpu
from jax.sharding import PartitionSpec as P

LANCZOS = 4
POWER = 4


def shifted(value, axis, steps):
    count = lax.axis_size(axis)
    pairs = [(source, (source + steps) % count) for source in range(count)]
    return lax.ppermute(value, axis, pairs)


def bond_sum(value):
    count = lax.axis_size("bond")
    if count & (count - 1):
        return lax.psum(value, "bond")
    step = 1
    while step < count:
        pairs = [(source, source ^ step) for source in range(count)]
        value = value + lax.ppermute(value, "bond", pairs)
        step *= 2
    return value


def apply_ham(vector, left, right, mask):
    rounded = (vector * mask).astype(jnp.bfloat16)
    inner = jnp.einsum("ij,wjk->wik", rounded, right, preferred_element_type=jnp.float32).astype(
        jnp.bfloat16
    )
    outer = jnp.einsum("wij,wjk->ik", left, inner, preferred_element_type=jnp.float32)
    return outer * mask


def gram_kernel(*refs):
    *vec_refs, out_ref = refs
    size = len(vec_refs)
    row = lax.broadcasted_iota(jnp.int32, out_ref.shape, 0)
    lane = lax.broadcasted_iota(jnp.int32, out_ref.shape, 1)
    out = jnp.zeros(out_ref.shape, jnp.float32)
    slot = 0
    for i in range(size):
        for j in range(i, size):
            total = jnp.sum(vec_refs[i][...] * vec_refs[j][...], axis=(0, 1), keepdims=True)
            out = jnp.where((row == 0) & (lane == slot), total, out)
            slot += 1
    out_ref[...] = out


def ritz_kernel(total_ref, out_ref):
    size = LANCZOS + 1
    shape = out_ref.shape
    slots = {}
    slot = 0
    for i in range(size):
        for j in range(i, size):
            slots[i, j] = slots[j, i] = slot
            slot += 1
    entries = {}
    for key in range(slot):
        entries[key] = jnp.full(shape, total_ref[0, key], jnp.float32)
    gram = [[entries[slots[i, j]] for j in range(size)] for i in range(size)]
    zero = jnp.zeros(shape, jnp.float32)

    def quad(first, second):
        acc = zero
        for i in range(size):
            for j in range(size):
                acc = acc + first[i] * gram[i][j] * second[j]
        return acc

    def combine(first, scale_first, second, scale_second):
        return [a * scale_first + b * scale_second for a, b in zip(first, second)]

    vector = [1.0 / jnp.sqrt(gram[0][0])] + [zero] * (size - 1)
    previous = [zero] * size
    beta_prev = zero
    alphas = []
    betas = []
    basis = []
    for step in range(LANCZOS):
        image = [zero] + vector[:-1]
        alpha = quad(image, vector)
        image = [w - alpha * v - beta_prev * p for w, v, p in zip(image, vector, previous)]
        alphas.append(alpha)
        basis.append(vector)
        if step + 1 < LANCZOS:
            beta = jnp.sqrt(quad(image, image))
            betas.append(beta)
            previous = vector
            vector = [w / beta for w in image]
            beta_prev = beta

    def tri_times(weights):
        rows = []
        for i in range(LANCZOS):
            acc = alphas[i] * weights[i]
            if i > 0:
                acc = acc + betas[i - 1] * weights[i - 1]
            if i + 1 < LANCZOS:
                acc = acc + betas[i] * weights[i + 1]
            rows.append(acc)
        return rows

    sigma = None
    for i in range(LANCZOS):
        bound = alphas[i]
        if i > 0:
            bound = bound + jnp.abs(betas[i - 1])
        if i + 1 < LANCZOS:
            bound = bound + jnp.abs(betas[i])
        sigma = bound if sigma is None else jnp.maximum(sigma, bound)
    weights = [zero + 1.0] + [zero] * (LANCZOS - 1)
    for turn in range(POWER):
        product = tri_times(weights)
        weights = [sigma * w - t for w, t in zip(weights, product)]
        norm = zero
        for w in weights:
            norm = norm + w * w
        norm = jnp.sqrt(norm)
        weights = [w / norm for w in weights]
    product = tri_times(weights)
    energy = zero
    for w, t in zip(weights, product):
        energy = energy + w * t
    coef = [c * weights[0] for c in basis[0]]
    for step in range(1, LANCZOS):
        coef = [c + weights[step] * b for c, b in zip(coef, basis[step])]
    lane = lax.broadcasted_iota(jnp.int32, shape, 1)
    out = zero
    for slot in range(LANCZOS):
        out = jnp.where(lane == slot, coef[slot], out)
    out_ref[...] = jnp.where(lane == LANCZOS, energy, out)


def lanczos(start, left, right, mask):
    krylov = [start * mask]
    for step in range(LANCZOS):
        krylov.append(apply_ham(krylov[-1], left, right, mask))
    tile = jax.ShapeDtypeStruct((8, 128), jnp.float32)
    local = pl.pallas_call(gram_kernel, out_shape=tile)(*krylov)
    total = bond_sum(local)
    out = pl.pallas_call(
        ritz_kernel, out_shape=tile, in_specs=[pl.BlockSpec(memory_space=pltpu.SMEM)]
    )(total)
    result = krylov[0] * out[0, 0]
    for step in range(1, LANCZOS):
        result = result + out[0, step] * krylov[step]
    return (result, out[0, LANCZOS])


def env_update(mixed, left_a):
    half_left = jnp.einsum(
        "wij,jk->wik", mixed, left_a, preferred_element_type=jnp.float32
    ).astype(jnp.bfloat16)
    return jnp.einsum(
        "ji,wjk->wik", left_a, half_left, preferred_element_type=jnp.float32
    ).astype(jnp.bfloat16)


def per_device(state, left_env, right_env, mpo_mix, block_sizes, ranks):
    blocks = lax.axis_size("bond")
    width = state.shape[-1]
    start = state[0, 0]
    left = left_env[0, 0]
    right = right_env[0, 0]
    index = jnp.arange(width, dtype=jnp.int32)
    live = (index < block_sizes[0, 0]).astype(jnp.float32)
    mask = live[:, None] * live[None, :]
    kept = (index < ranks[0, 0]).astype(jnp.float32)
    left_mix = jnp.einsum(
        "wu,uij->wij", mpo_mix, left.astype(jnp.float32), precision=lax.Precision.HIGHEST
    ).astype(jnp.bfloat16)
    right_mix = jnp.einsum(
        "wu,uij->wij", mpo_mix, right.astype(jnp.float32), precision=lax.Precision.HIGHEST
    ).astype(jnp.bfloat16)
    left_mix_got = shifted(left_mix, "seg", 1)
    right_mix_got = shifted(right_mix, "seg", -1)
    psi_one, unused = lanczos(start, left, right, mask)
    scaled = psi_one * math.sqrt(blocks * width)
    left_a = (scaled * kept[None, :]).astype(jnp.bfloat16)
    right_a = (scaled * kept[:, None]).astype(jnp.bfloat16)
    left_a_got = shifted(left_a, "seg", 1)
    right_a_got = shifted(right_a, "seg", -1)
    left_in = env_update(left_mix_got, left_a_got)
    right_in = env_update(right_mix_got, right_a_got.T)
    psi_two, energy = lanczos(psi_one, left_in, right_in, mask)
    ground = psi_two * math.sqrt(blocks * width * width)
    return (ground[None, None], jnp.reshape(energy, (1,)))


def solution(mesh):
    in_specs = (
        P("seg", "bond", None, None),
        P("seg", "bond", None, None, None),
        P("seg", "bond", None, None, None),
        P(),
        P("seg", "bond"),
        P("seg", "bond"),
    )
    out_specs = (P("seg", "bond", None, None), P("seg"))
    return jax.shard_map(
        per_device, mesh=mesh, in_specs=in_specs, out_specs=out_specs, check_vma=False
    )
```

```python
import functools
import math

import jax
import jax.numpy as jnp
from jax import lax
from jax.experimental import pallas as pl
from jax.experimental.pallas import tpu as pltpu
from jax.sharding import PartitionSpec as P

LANCZOS = 4
POWER = 4


def shifted(value, axis, steps):
    count = lax.axis_size(axis)
    pairs = [(source, (source + steps) % count) for source in range(count)]
    return lax.ppermute(value, axis, pairs)


def bond_sum(value):
    count = lax.axis_size("bond")
    if count & (count - 1):
        return lax.psum(value, "bond")
    step = 1
    while step < count:
        pairs = [(source, source ^ step) for source in range(count)]
        value = value + lax.ppermute(value, "bond", pairs)
        step *= 2
    return value


def apply_ham(vector, left, right, mask):
    rounded = (vector * mask).astype(jnp.bfloat16)
    inner = jnp.einsum("ij,wjk->wik", rounded, right, preferred_element_type=jnp.float32).astype(
        jnp.bfloat16
    )
    outer = jnp.einsum("wij,wjk->ik", left, inner, preferred_element_type=jnp.float32)
    return outer * mask


def gram_kernel(*refs):
    *vec_refs, out_ref = refs
    size = len(vec_refs)
    row = lax.broadcasted_iota(jnp.int32, out_ref.shape, 0)
    lane = lax.broadcasted_iota(jnp.int32, out_ref.shape, 1)
    out = jnp.zeros(out_ref.shape, jnp.float32)
    slot = 0
    for i in range(size):
        for j in range(i, size):
            total = jnp.sum(vec_refs[i][...] * vec_refs[j][...], axis=(0, 1), keepdims=True)
            out = jnp.where((row == 0) & (lane == slot), total, out)
            slot += 1
    out_ref[...] = out


def ritz_kernel(total_ref, out_ref):
    size = LANCZOS + 1
    shape = out_ref.shape
    slots = {}
    slot = 0
    for i in range(size):
        for j in range(i, size):
            slots[i, j] = slots[j, i] = slot
            slot += 1
    entries = {}
    for key in range(slot):
        entries[key] = jnp.full(shape, total_ref[0, key], jnp.float32)
    gram = [[entries[slots[i, j]] for j in range(size)] for i in range(size)]
    zero = jnp.zeros(shape, jnp.float32)

    def quad(first, second):
        acc = zero
        for i in range(size):
            for j in range(size):
                acc = acc + first[i] * gram[i][j] * second[j]
        return acc

    def combine(first, scale_first, second, scale_second):
        return [a * scale_first + b * scale_second for a, b in zip(first, second)]

    vector = [1.0 / jnp.sqrt(gram[0][0])] + [zero] * (size - 1)
    previous = [zero] * size
    beta_prev = zero
    alphas = []
    betas = []
    basis = []
    for step in range(LANCZOS):
        image = [zero] + vector[:-1]
        alpha = quad(image, vector)
        image = [w - alpha * v - beta_prev * p for w, v, p in zip(image, vector, previous)]
        alphas.append(alpha)
        basis.append(vector)
        if step + 1 < LANCZOS:
            beta = jnp.sqrt(quad(image, image))
            betas.append(beta)
            previous = vector
            vector = [w / beta for w in image]
            beta_prev = beta

    def tri_times(weights):
        rows = []
        for i in range(LANCZOS):
            acc = alphas[i] * weights[i]
            if i > 0:
                acc = acc + betas[i - 1] * weights[i - 1]
            if i + 1 < LANCZOS:
                acc = acc + betas[i] * weights[i + 1]
            rows.append(acc)
        return rows

    sigma = None
    for i in range(LANCZOS):
        bound = alphas[i]
        if i > 0:
            bound = bound + jnp.abs(betas[i - 1])
        if i + 1 < LANCZOS:
            bound = bound + jnp.abs(betas[i])
        sigma = bound if sigma is None else jnp.maximum(sigma, bound)
    weights = [zero + 1.0] + [zero] * (LANCZOS - 1)
    for turn in range(POWER):
        product = tri_times(weights)
        weights = [sigma * w - t for w, t in zip(weights, product)]
        norm = zero
        for w in weights:
            norm = norm + w * w
        norm = jnp.sqrt(norm)
        weights = [w / norm for w in weights]
    product = tri_times(weights)
    energy = zero
    for w, t in zip(weights, product):
        energy = energy + w * t
    coef = [c * weights[0] for c in basis[0]]
    for step in range(1, LANCZOS):
        coef = [c + weights[step] * b for c, b in zip(coef, basis[step])]
    lane = lax.broadcasted_iota(jnp.int32, shape, 1)
    out = zero
    for slot in range(LANCZOS):
        out = jnp.where(lane == slot, coef[slot], out)
    out_ref[...] = jnp.where(lane == LANCZOS, energy, out)


def combine_kernel(coef_ref, *refs, scale):
    *vec_refs, out_ref = refs
    acc = vec_refs[0][...] * coef_ref[0, 0]
    for step in range(1, len(vec_refs)):
        acc = acc + coef_ref[0, step] * vec_refs[step][...]
    if scale is not None:
        acc = acc * scale
    out_ref[...] = acc


def lanczos(start, left, right, mask, scale=None):
    krylov = [start * mask]
    for step in range(LANCZOS):
        krylov.append(apply_ham(krylov[-1], left, right, mask))
    tile = jax.ShapeDtypeStruct((8, 128), jnp.float32)
    local = pl.pallas_call(gram_kernel, out_shape=tile)(*krylov)
    total = bond_sum(local)
    out = pl.pallas_call(
        ritz_kernel, out_shape=tile, in_specs=[pl.BlockSpec(memory_space=pltpu.SMEM)]
    )(total)
    vec_spec = pl.BlockSpec(memory_space=pltpu.VMEM)
    result = pl.pallas_call(
        functools.partial(combine_kernel, scale=scale),
        out_shape=jax.ShapeDtypeStruct(start.shape, jnp.float32),
        in_specs=[pl.BlockSpec(memory_space=pltpu.SMEM)] + [vec_spec] * LANCZOS,
    )(out, *krylov[:LANCZOS])
    return (result, krylov[LANCZOS], local, out[0, LANCZOS])


def env_update(mixed, left_a):
    half_left = jnp.einsum(
        "wij,jk->wik", mixed, left_a, preferred_element_type=jnp.float32
    ).astype(jnp.bfloat16)
    return jnp.einsum(
        "ji,wjk->wik", left_a, half_left, preferred_element_type=jnp.float32
    ).astype(jnp.bfloat16)


def per_device(state, left_env, right_env, mpo_mix, block_sizes, ranks):
    blocks = lax.axis_size("bond")
    width = state.shape[-1]
    start = state[0, 0]
    left = left_env[0, 0]
    right = right_env[0, 0]
    index = jnp.arange(width, dtype=jnp.int32)
    live = (index < block_sizes[0, 0]).astype(jnp.float32)
    mask = live[:, None] * live[None, :]
    kept = (index < ranks[0, 0]).astype(jnp.float32)
    left_got = shifted(left, "seg", 1)
    right_got = shifted(right, "seg", -1)
    psi_one, last, local, unused = lanczos(start, left, right, mask)
    left_got, right_got, last = lax.optimization_barrier((left_got, right_got, last))
    left_mix = jnp.einsum(
        "wu,uij->wij", mpo_mix, left_got.astype(jnp.float32), precision=lax.Precision.HIGHEST
    ).astype(jnp.bfloat16)
    right_mix = jnp.einsum(
        "wu,uij->wij", mpo_mix, right_got.astype(jnp.float32), precision=lax.Precision.HIGHEST
    ).astype(jnp.bfloat16)
    scaled = psi_one * math.sqrt(blocks * width)
    left_a = (scaled * kept[None, :]).astype(jnp.bfloat16)
    right_a = (scaled * kept[:, None]).astype(jnp.bfloat16)
    left_a_got = shifted(left_a, "seg", 1)
    right_a_got = shifted(right_a, "seg", -1)
    left_in = env_update(left_mix, left_a_got)
    right_in = env_update(right_mix, right_a_got.T)
    ground, last, local, energy = lanczos(
        psi_one, left_in, right_in, mask, math.sqrt(blocks * width * width)
    )
    return (ground[None, None], jnp.reshape(energy, (1,)))


def solution(mesh):
    in_specs = (
        P("seg", "bond", None, None),
        P("seg", "bond", None, None, None),
        P("seg", "bond", None, None, None),
        P(),
        P("seg", "bond"),
        P("seg", "bond"),
    )
    out_specs = (P("seg", "bond", None, None), P("seg"))
    return jax.shard_map(
        per_device, mesh=mesh, in_specs=in_specs, out_specs=out_specs, check_vma=False
    )
```

```python
import functools
import math

import jax
import jax.numpy as jnp
from jax import lax
from jax.experimental import pallas as pl
from jax.experimental.pallas import tpu as pltpu
from jax.sharding import PartitionSpec as P

LANCZOS = 4
POWER = 4


def shifted(value, axis, steps):
    count = lax.axis_size(axis)
    pairs = [(source, (source + steps) % count) for source in range(count)]
    return lax.ppermute(value, axis, pairs)


def bond_sum(value):
    count = lax.axis_size("bond")
    if count & (count - 1):
        return lax.psum(value, "bond")
    step = 1
    while step < count:
        pairs = [(source, source ^ step) for source in range(count)]
        value = value + lax.ppermute(value, "bond", pairs)
        step *= 2
    return value


def apply_ham(vector, left, right, mask):
    rounded = (vector * mask).astype(jnp.bfloat16)
    inner = jnp.einsum("ij,wjk->wik", rounded, right, preferred_element_type=jnp.float32).astype(
        jnp.bfloat16
    )
    outer = jnp.einsum("wij,wjk->ik", left, inner, preferred_element_type=jnp.float32)
    return outer * mask


def gram_kernel(head_ref, *refs):
    *vec_refs, out_ref = refs
    size = len(vec_refs)
    row = lax.broadcasted_iota(jnp.int32, out_ref.shape, 0)
    lane = lax.broadcasted_iota(jnp.int32, out_ref.shape, 1)
    out = jnp.zeros(out_ref.shape, jnp.float32)
    slot = 0
    for i in range(size):
        for j in range(i, size):
            if i == 0 and j == 0:
                head = head_ref[...]
                total = jnp.sum(head * head, axis=(0, 1), keepdims=True)
            else:
                total = jnp.sum(vec_refs[i][...] * vec_refs[j][...], axis=(0, 1), keepdims=True)
            out = jnp.where((row == 0) & (lane == slot), total, out)
            slot += 1
    out_ref[...] = out


def ritz_kernel(total_ref, out_ref):
    size = LANCZOS + 1
    shape = out_ref.shape
    slots = {}
    slot = 0
    for i in range(size):
        for j in range(i, size):
            slots[i, j] = slots[j, i] = slot
            slot += 1
    entries = {}
    for key in range(slot):
        entries[key] = jnp.full(shape, total_ref[0, key], jnp.float32)
    gram = [[entries[slots[i, j]] for j in range(size)] for i in range(size)]
    zero = jnp.zeros(shape, jnp.float32)

    def quad(first, second):
        acc = zero
        for i in range(size):
            for j in range(size):
                acc = acc + first[i] * gram[i][j] * second[j]
        return acc

    def combine(first, scale_first, second, scale_second):
        return [a * scale_first + b * scale_second for a, b in zip(first, second)]

    vector = [1.0 / jnp.sqrt(gram[0][0])] + [zero] * (size - 1)
    previous = [zero] * size
    beta_prev = zero
    alphas = []
    betas = []
    basis = []
    for step in range(LANCZOS):
        image = [zero] + vector[:-1]
        alpha = quad(image, vector)
        image = [w - alpha * v - beta_prev * p for w, v, p in zip(image, vector, previous)]
        alphas.append(alpha)
        basis.append(vector)
        if step + 1 < LANCZOS:
            beta = jnp.sqrt(quad(image, image))
            betas.append(beta)
            previous = vector
            vector = [w / beta for w in image]
            beta_prev = beta

    def tri_times(weights):
        rows = []
        for i in range(LANCZOS):
            acc = alphas[i] * weights[i]
            if i > 0:
                acc = acc + betas[i - 1] * weights[i - 1]
            if i + 1 < LANCZOS:
                acc = acc + betas[i] * weights[i + 1]
            rows.append(acc)
        return rows

    sigma = None
    for i in range(LANCZOS):
        bound = alphas[i]
        if i > 0:
            bound = bound + jnp.abs(betas[i - 1])
        if i + 1 < LANCZOS:
            bound = bound + jnp.abs(betas[i])
        sigma = bound if sigma is None else jnp.maximum(sigma, bound)
    weights = [zero + 1.0] + [zero] * (LANCZOS - 1)
    for turn in range(POWER):
        product = tri_times(weights)
        weights = [sigma * w - t for w, t in zip(weights, product)]
        norm = zero
        for w in weights:
            norm = norm + w * w
        norm = jnp.sqrt(norm)
        weights = [w / norm for w in weights]
    product = tri_times(weights)
    energy = zero
    for w, t in zip(weights, product):
        energy = energy + w * t
    coef = [c * weights[0] for c in basis[0]]
    for step in range(1, LANCZOS):
        coef = [c + weights[step] * b for c, b in zip(coef, basis[step])]
    lane = lax.broadcasted_iota(jnp.int32, shape, 1)
    out = zero
    for slot in range(LANCZOS):
        out = jnp.where(lane == slot, coef[slot], out)
    out_ref[...] = jnp.where(lane == LANCZOS, energy, out)


def combine_kernel(coef_ref, head_ref, *refs, scale):
    *vec_refs, out_ref = refs
    rows, cols = vec_refs[0].shape
    acc = vec_refs[0][...] * coef_ref[0, 0]
    for step in range(1, len(vec_refs)):
        acc = acc + coef_ref[0, step] * vec_refs[step][...]
    if scale is not None:
        acc = acc * scale
    if head_ref.shape != vec_refs[0].shape:
        rest = head_ref[...] * coef_ref[0, 0]
        if scale is not None:
            rest = rest * scale
        out_ref[...] = rest
    out_ref[:rows, :cols] = acc


def lanczos(start, left, right, mask, scale=None, cut=None):
    head = start * mask
    if cut is None:
        base, live = head, mask
    else:
        base, live = head[:cut, :cut], mask[:cut, :cut]
    krylov = [base]
    for step in range(LANCZOS):
        krylov.append(apply_ham(krylov[-1], left, right, live))
    tile = jax.ShapeDtypeStruct((8, 128), jnp.float32)
    local = pl.pallas_call(gram_kernel, out_shape=tile)(head, *krylov)
    total = bond_sum(local)
    out = pl.pallas_call(
        ritz_kernel, out_shape=tile, in_specs=[pl.BlockSpec(memory_space=pltpu.SMEM)]
    )(total)
    vec_spec = pl.BlockSpec(memory_space=pltpu.VMEM)
    result = pl.pallas_call(
        functools.partial(combine_kernel, scale=scale),
        out_shape=jax.ShapeDtypeStruct(head.shape, jnp.float32),
        in_specs=[pl.BlockSpec(memory_space=pltpu.SMEM)] + [vec_spec] * (LANCZOS + 1),
    )(out, head, *krylov[:LANCZOS])
    return (result, krylov[LANCZOS], local, out[0, LANCZOS])


def env_update(mixed, left_a):
    half_left = jnp.einsum(
        "wij,jk->wik", mixed, left_a, preferred_element_type=jnp.float32
    ).astype(jnp.bfloat16)
    return jnp.einsum(
        "ji,wjk->wik", left_a, half_left, preferred_element_type=jnp.float32
    ).astype(jnp.bfloat16)


def per_device(state, left_env, right_env, mpo_mix, block_sizes, ranks):
    blocks = lax.axis_size("bond")
    width = state.shape[-1]
    start = state[0, 0]
    left = left_env[0, 0]
    right = right_env[0, 0]
    index = jnp.arange(width, dtype=jnp.int32)
    live = (index < block_sizes[0, 0]).astype(jnp.float32)
    mask = live[:, None] * live[None, :]
    kept = (index < ranks[0, 0]).astype(jnp.float32)
    left_got = shifted(left, "seg", 1)
    right_got = shifted(right, "seg", -1)
    psi_one, last, local, unused = lanczos(start, left, right, mask)
    left_got, right_got, last = lax.optimization_barrier((left_got, right_got, last))
    left_mix = jnp.einsum(
        "wu,uij->wij", mpo_mix, left_got.astype(jnp.float32), precision=lax.Precision.HIGHEST
    ).astype(jnp.bfloat16)
    right_mix = jnp.einsum(
        "wu,uij->wij", mpo_mix, right_got.astype(jnp.float32), precision=lax.Precision.HIGHEST
    ).astype(jnp.bfloat16)
    scaled = psi_one * math.sqrt(blocks * width)
    cut = width // 2
    left_a = (scaled[:, :cut] * kept[None, :cut]).astype(jnp.bfloat16)
    right_a = (scaled[:cut, :] * kept[:cut, None]).astype(jnp.bfloat16)
    left_a_got = shifted(left_a, "seg", 1)
    right_a_got = shifted(right_a, "seg", -1)
    left_in = env_update(left_mix, left_a_got)
    right_in = env_update(right_mix, right_a_got.T)
    ground, last, local, energy = lanczos(
        psi_one, left_in, right_in, mask, math.sqrt(blocks * width * width), cut
    )
    return (ground[None, None], jnp.reshape(energy, (1,)))


def solution(mesh):
    in_specs = (
        P("seg", "bond", None, None),
        P("seg", "bond", None, None, None),
        P("seg", "bond", None, None, None),
        P(),
        P("seg", "bond"),
        P("seg", "bond"),
    )
    out_specs = (P("seg", "bond", None, None), P("seg"))
    return jax.shard_map(
        per_device, mesh=mesh, in_specs=in_specs, out_specs=out_specs, check_vma=False
    )
```

```python
import functools
import math

import jax
import jax.numpy as jnp
from jax import lax
from jax.experimental import pallas as pl
from jax.experimental.pallas import tpu as pltpu
from jax.sharding import PartitionSpec as P

LANCZOS = 4
POWER = 4


def shifted(value, axis, steps):
    count = lax.axis_size(axis)
    pairs = [(source, (source + steps) % count) for source in range(count)]
    return lax.ppermute(value, axis, pairs)


def bond_sum(value, hooks=None):
    hooks = hooks or {}
    count = lax.axis_size("bond")
    if count & (count - 1):
        for index in sorted(hooks):
            value = hooks[index](value)
        return lax.psum(value, "bond")
    rounds = count.bit_length() - 1
    for index in range(rounds):
        if index in hooks:
            value = hooks[index](value)
        pairs = [(source, source ^ (1 << index)) for source in range(count)]
        value = value + lax.ppermute(value, "bond", pairs)
    for index in sorted(hooks):
        if index >= rounds:
            value = hooks[index](value)
    return value


def apply_ham(vector, left, right, mask):
    rounded = (vector * mask).astype(jnp.bfloat16)
    inner = jnp.einsum("ij,wjk->wik", rounded, right, preferred_element_type=jnp.float32).astype(
        jnp.bfloat16
    )
    outer = jnp.einsum("wij,wjk->ik", left, inner, preferred_element_type=jnp.float32)
    return outer * mask


def gram_kernel(head_ref, *refs):
    *vec_refs, out_ref = refs
    size = len(vec_refs)
    row = lax.broadcasted_iota(jnp.int32, out_ref.shape, 0)
    lane = lax.broadcasted_iota(jnp.int32, out_ref.shape, 1)
    out = jnp.zeros(out_ref.shape, jnp.float32)
    slot = 0
    for i in range(size):
        for j in range(i, size):
            if i == 0 and j == 0:
                head = head_ref[...]
                total = jnp.sum(head * head, axis=(0, 1), keepdims=True)
            else:
                total = jnp.sum(vec_refs[i][...] * vec_refs[j][...], axis=(0, 1), keepdims=True)
            out = jnp.where((row == 0) & (lane == slot), total, out)
            slot += 1
    out_ref[...] = out


def ritz_kernel(total_ref, out_ref):
    size = LANCZOS + 1
    shape = out_ref.shape
    slots = {}
    slot = 0
    for i in range(size):
        for j in range(i, size):
            slots[i, j] = slots[j, i] = slot
            slot += 1
    entries = {}
    for key in range(slot):
        entries[key] = jnp.full(shape, total_ref[0, key], jnp.float32)
    gram = [[entries[slots[i, j]] for j in range(size)] for i in range(size)]
    zero = jnp.zeros(shape, jnp.float32)

    def quad(first, second):
        acc = zero
        for i in range(size):
            for j in range(size):
                acc = acc + first[i] * gram[i][j] * second[j]
        return acc

    def combine(first, scale_first, second, scale_second):
        return [a * scale_first + b * scale_second for a, b in zip(first, second)]

    vector = [1.0 / jnp.sqrt(gram[0][0])] + [zero] * (size - 1)
    previous = [zero] * size
    beta_prev = zero
    alphas = []
    betas = []
    basis = []
    for step in range(LANCZOS):
        image = [zero] + vector[:-1]
        alpha = quad(image, vector)
        image = [w - alpha * v - beta_prev * p for w, v, p in zip(image, vector, previous)]
        alphas.append(alpha)
        basis.append(vector)
        if step + 1 < LANCZOS:
            beta = jnp.sqrt(quad(image, image))
            betas.append(beta)
            previous = vector
            vector = [w / beta for w in image]
            beta_prev = beta

    def tri_times(weights):
        rows = []
        for i in range(LANCZOS):
            acc = alphas[i] * weights[i]
            if i > 0:
                acc = acc + betas[i - 1] * weights[i - 1]
            if i + 1 < LANCZOS:
                acc = acc + betas[i] * weights[i + 1]
            rows.append(acc)
        return rows

    sigma = None
    for i in range(LANCZOS):
        bound = alphas[i]
        if i > 0:
            bound = bound + jnp.abs(betas[i - 1])
        if i + 1 < LANCZOS:
            bound = bound + jnp.abs(betas[i])
        sigma = bound if sigma is None else jnp.maximum(sigma, bound)
    weights = [zero + 1.0] + [zero] * (LANCZOS - 1)
    for turn in range(POWER):
        product = tri_times(weights)
        weights = [sigma * w - t for w, t in zip(weights, product)]
        norm = zero
        for w in weights:
            norm = norm + w * w
        norm = jnp.sqrt(norm)
        weights = [w / norm for w in weights]
    product = tri_times(weights)
    energy = zero
    for w, t in zip(weights, product):
        energy = energy + w * t
    coef = [c * weights[0] for c in basis[0]]
    for step in range(1, LANCZOS):
        coef = [c + weights[step] * b for c, b in zip(coef, basis[step])]
    lane = lax.broadcasted_iota(jnp.int32, shape, 1)
    out = zero
    for slot in range(LANCZOS):
        out = jnp.where(lane == slot, coef[slot], out)
    out_ref[...] = jnp.where(lane == LANCZOS, energy, out)


def combine_kernel(coef_ref, head_ref, *refs, scale):
    *vec_refs, out_ref = refs
    rows, cols = vec_refs[0].shape
    acc = vec_refs[0][...] * coef_ref[0, 0]
    for step in range(1, len(vec_refs)):
        acc = acc + coef_ref[0, step] * vec_refs[step][...]
    if scale is not None:
        acc = acc * scale
    if head_ref.shape != vec_refs[0].shape:
        rest = head_ref[...] * coef_ref[0, 0]
        if scale is not None:
            rest = rest * scale
        out_ref[...] = rest
    out_ref[:rows, :cols] = acc


def lanczos(start, left, right, mask, scale=None, cut=None, hooks=None):
    head = start * mask
    if cut is None:
        base, live = head, mask
    else:
        base, live = head[:cut, :cut], mask[:cut, :cut]
    krylov = [base]
    for step in range(LANCZOS):
        krylov.append(apply_ham(krylov[-1], left, right, live))
    tile = jax.ShapeDtypeStruct((8, 128), jnp.float32)
    local = pl.pallas_call(gram_kernel, out_shape=tile)(head, *krylov)
    total = bond_sum(local, hooks)
    out = pl.pallas_call(
        ritz_kernel, out_shape=tile, in_specs=[pl.BlockSpec(memory_space=pltpu.SMEM)]
    )(total)
    vec_spec = pl.BlockSpec(memory_space=pltpu.VMEM)
    result = pl.pallas_call(
        functools.partial(combine_kernel, scale=scale),
        out_shape=jax.ShapeDtypeStruct(head.shape, jnp.float32),
        in_specs=[pl.BlockSpec(memory_space=pltpu.SMEM)] + [vec_spec] * (LANCZOS + 1),
    )(out, head, *krylov[:LANCZOS])
    return (result, out[0, LANCZOS])


def env_update(mixed, left_a):
    half_left = jnp.einsum(
        "wij,jk->wik", mixed, left_a, preferred_element_type=jnp.float32
    ).astype(jnp.bfloat16)
    return jnp.einsum(
        "ji,wjk->wik", left_a, half_left, preferred_element_type=jnp.float32
    ).astype(jnp.bfloat16)


def per_device(state, left_env, right_env, mpo_mix, block_sizes, ranks):
    blocks = lax.axis_size("bond")
    width = state.shape[-1]
    start = state[0, 0]
    left = left_env[0, 0]
    right = right_env[0, 0]
    index = jnp.arange(width, dtype=jnp.int32)
    live = (index < block_sizes[0, 0]).astype(jnp.float32)
    mask = live[:, None] * live[None, :]
    kept = (index < ranks[0, 0]).astype(jnp.float32)
    left_got = shifted(left, "seg", 1)
    right_got = shifted(right, "seg", -1)

    def mixed(env):
        return jnp.einsum(
            "wu,uij->wij", mpo_mix, env.astype(jnp.float32), precision=lax.Precision.HIGHEST
        ).astype(jnp.bfloat16)

    held = {}

    def take_envs(value):
        value, held["left"], held["right"] = lax.optimization_barrier((value, left_got, right_got))
        return value

    def mix_left(value):
        value, held["left"] = lax.optimization_barrier((value, mixed(held["left"])))
        return value

    def mix_right(value):
        value, held["right"] = lax.optimization_barrier((value, mixed(held["right"])))
        return value

    hooks = {1: take_envs, 3: mix_left, 4: mix_right}
    psi_one, unused = lanczos(start, left, right, mask, hooks=hooks)
    left_mix, right_mix = held["left"], held["right"]
    scaled = psi_one * math.sqrt(blocks * width)
    cut = width // 2
    left_a = (scaled[:, :cut] * kept[None, :cut]).astype(jnp.bfloat16)
    right_a = (scaled[:cut, :] * kept[:cut, None]).astype(jnp.bfloat16)
    left_a_got = shifted(left_a, "seg", 1)
    right_a_got = shifted(right_a, "seg", -1)
    left_in = env_update(left_mix, left_a_got)
    right_in = env_update(right_mix, right_a_got.T)
    ground, energy = lanczos(
        psi_one, left_in, right_in, mask, math.sqrt(blocks * width * width), cut
    )
    return (ground[None, None], jnp.reshape(energy, (1,)))


def solution(mesh):
    in_specs = (
        P("seg", "bond", None, None),
        P("seg", "bond", None, None, None),
        P("seg", "bond", None, None, None),
        P(),
        P("seg", "bond"),
        P("seg", "bond"),
    )
    out_specs = (P("seg", "bond", None, None), P("seg"))
    return jax.shard_map(
        per_device, mesh=mesh, in_specs=in_specs, out_specs=out_specs, check_vma=False
    )
```

```python
import functools
import math

import jax
import jax.numpy as jnp
from jax import lax
from jax.experimental import pallas as pl
from jax.experimental.pallas import tpu as pltpu
from jax.sharding import PartitionSpec as P

LANCZOS = 4
POWER = 4


def shifted(value, axis, steps):
    count = lax.axis_size(axis)
    pairs = [(source, (source + steps) % count) for source in range(count)]
    return lax.ppermute(value, axis, pairs)


def bond_sum(value, hooks=None):
    hooks = hooks or {}
    count = lax.axis_size("bond")
    if count & (count - 1):
        for index in sorted(hooks):
            value = hooks[index](value)
        return lax.psum(value, "bond")
    rounds = count.bit_length() - 1
    for index in range(rounds):
        if index in hooks:
            value = hooks[index](value)
        pairs = [(source, source ^ (1 << index)) for source in range(count)]
        value = value + lax.ppermute(value, "bond", pairs)
    for index in sorted(hooks):
        if index >= rounds:
            value = hooks[index](value)
    return value


def krylov_kernel(start_ref, mask_ref, left_ref, right_ref, krylov_ref, gram_ref):
    channels, n = left_ref.shape[0], left_ref.shape[-1]
    head = start_ref[...] * mask_ref[...]
    live = mask_ref[:n, :n]
    krylov_ref[0] = head[:n, :n]
    for step in range(LANCZOS):
        rounded = (krylov_ref[step] * live).astype(jnp.bfloat16)
        krylov_ref[step + 1] = jnp.zeros((n, n), jnp.float32)

        def channel(w, carry, rounded=rounded, step=step):
            inner = jnp.dot(rounded, right_ref[w], preferred_element_type=jnp.float32)
            krylov_ref[step + 1] += jnp.dot(
                left_ref[w], inner.astype(jnp.bfloat16), preferred_element_type=jnp.float32
            )
            return carry

        lax.fori_loop(0, channels, channel, 0)
        krylov_ref[step + 1] = krylov_ref[step + 1] * live
    row = lax.broadcasted_iota(jnp.int32, gram_ref.shape, 0)
    lane = lax.broadcasted_iota(jnp.int32, gram_ref.shape, 1)
    out = jnp.zeros(gram_ref.shape, jnp.float32)
    slot = 0
    for i in range(LANCZOS + 1):
        for j in range(i, LANCZOS + 1):
            if i == 0 and j == 0:
                total = jnp.sum(head * head, axis=(0, 1), keepdims=True)
            else:
                total = jnp.sum(krylov_ref[i] * krylov_ref[j], axis=(0, 1), keepdims=True)
            out = jnp.where((row == 0) & (lane == slot), total, out)
            slot += 1
    gram_ref[...] = out


def ritz_kernel(total_ref, out_ref):
    size = LANCZOS + 1
    shape = out_ref.shape
    slots = {}
    slot = 0
    for i in range(size):
        for j in range(i, size):
            slots[i, j] = slots[j, i] = slot
            slot += 1
    entries = {}
    for key in range(slot):
        entries[key] = jnp.full(shape, total_ref[0, key], jnp.float32)
    gram = [[entries[slots[i, j]] for j in range(size)] for i in range(size)]
    zero = jnp.zeros(shape, jnp.float32)

    def quad(first, second):
        acc = zero
        for i in range(size):
            for j in range(size):
                acc = acc + first[i] * gram[i][j] * second[j]
        return acc

    def combine(first, scale_first, second, scale_second):
        return [a * scale_first + b * scale_second for a, b in zip(first, second)]

    vector = [1.0 / jnp.sqrt(gram[0][0])] + [zero] * (size - 1)
    previous = [zero] * size
    beta_prev = zero
    alphas = []
    betas = []
    basis = []
    for step in range(LANCZOS):
        image = [zero] + vector[:-1]
        alpha = quad(image, vector)
        image = [w - alpha * v - beta_prev * p for w, v, p in zip(image, vector, previous)]
        alphas.append(alpha)
        basis.append(vector)
        if step + 1 < LANCZOS:
            beta = jnp.sqrt(quad(image, image))
            betas.append(beta)
            previous = vector
            vector = [w / beta for w in image]
            beta_prev = beta

    def tri_times(weights):
        rows = []
        for i in range(LANCZOS):
            acc = alphas[i] * weights[i]
            if i > 0:
                acc = acc + betas[i - 1] * weights[i - 1]
            if i + 1 < LANCZOS:
                acc = acc + betas[i] * weights[i + 1]
            rows.append(acc)
        return rows

    sigma = None
    for i in range(LANCZOS):
        bound = alphas[i]
        if i > 0:
            bound = bound + jnp.abs(betas[i - 1])
        if i + 1 < LANCZOS:
            bound = bound + jnp.abs(betas[i])
        sigma = bound if sigma is None else jnp.maximum(sigma, bound)
    weights = [zero + 1.0] + [zero] * (LANCZOS - 1)
    for turn in range(POWER):
        product = tri_times(weights)
        weights = [sigma * w - t for w, t in zip(weights, product)]
        norm = zero
        for w in weights:
            norm = norm + w * w
        norm = jnp.sqrt(norm)
        weights = [w / norm for w in weights]
    product = tri_times(weights)
    energy = zero
    for w, t in zip(weights, product):
        energy = energy + w * t
    coef = [c * weights[0] for c in basis[0]]
    for step in range(1, LANCZOS):
        coef = [c + weights[step] * b for c, b in zip(coef, basis[step])]
    lane = lax.broadcasted_iota(jnp.int32, shape, 1)
    out = zero
    for slot in range(LANCZOS):
        out = jnp.where(lane == slot, coef[slot], out)
    out_ref[...] = jnp.where(lane == LANCZOS, energy, out)


def combine_kernel(coef_ref, start_ref, mask_ref, krylov_ref, out_ref, *, scale):
    n = krylov_ref.shape[-1]
    head = start_ref[...] * mask_ref[...]
    acc = head[:n, :n] * coef_ref[0, 0]
    for step in range(1, LANCZOS):
        acc = acc + coef_ref[0, step] * krylov_ref[step]
    if scale is not None:
        acc = acc * scale
    if head.shape != (n, n):
        rest = head * coef_ref[0, 0]
        if scale is not None:
            rest = rest * scale
        out_ref[...] = rest
    out_ref[:n, :n] = acc


def lanczos(start, left, right, mask, scale=None, hooks=None):
    n = left.shape[-1]
    tile = jax.ShapeDtypeStruct((8, 128), jnp.float32)
    krylov, local = pl.pallas_call(
        krylov_kernel,
        out_shape=(jax.ShapeDtypeStruct((LANCZOS + 1, n, n), jnp.float32), tile),
    )(start, mask, left, right)
    total = bond_sum(local, hooks)
    smem = pl.BlockSpec(memory_space=pltpu.SMEM)
    out = pl.pallas_call(ritz_kernel, out_shape=tile, in_specs=[smem])(total)
    vec_spec = pl.BlockSpec(memory_space=pltpu.VMEM)
    result = pl.pallas_call(
        functools.partial(combine_kernel, scale=scale),
        out_shape=jax.ShapeDtypeStruct(start.shape, jnp.float32),
        in_specs=[smem, vec_spec, vec_spec, vec_spec],
    )(out, start, mask, krylov)
    return (result, out[0, LANCZOS])


def env_update(mixed, left_a):
    half_left = jnp.einsum(
        "wij,jk->wik", mixed, left_a, preferred_element_type=jnp.float32
    ).astype(jnp.bfloat16)
    return jnp.einsum(
        "ji,wjk->wik", left_a, half_left, preferred_element_type=jnp.float32
    ).astype(jnp.bfloat16)


def per_device(state, left_env, right_env, mpo_mix, block_sizes, ranks):
    blocks = lax.axis_size("bond")
    width = state.shape[-1]
    start = state[0, 0]
    left = left_env[0, 0]
    right = right_env[0, 0]
    index = jnp.arange(width, dtype=jnp.int32)
    live = (index < block_sizes[0, 0]).astype(jnp.float32)
    mask = live[:, None] * live[None, :]
    kept = (index < ranks[0, 0]).astype(jnp.float32)
    left_got = shifted(left, "seg", 1)
    right_got = shifted(right, "seg", -1)

    def mixed(env):
        return jnp.einsum(
            "wu,uij->wij", mpo_mix, env.astype(jnp.float32), precision=lax.Precision.HIGHEST
        ).astype(jnp.bfloat16)

    held = {}

    def take_envs(value):
        value, held["left"], held["right"] = lax.optimization_barrier((value, left_got, right_got))
        return value

    def mix_left(value):
        value, held["left"] = lax.optimization_barrier((value, mixed(held["left"])))
        return value

    def mix_right(value):
        value, held["right"] = lax.optimization_barrier((value, mixed(held["right"])))
        return value

    hooks = {1: take_envs, 3: mix_left, 4: mix_right}
    psi_one, unused = lanczos(start, left, right, mask, hooks=hooks)
    left_mix, right_mix = held["left"], held["right"]
    scaled = psi_one * math.sqrt(blocks * width)
    cut = width // 2
    left_a = (scaled[:, :cut] * kept[None, :cut]).astype(jnp.bfloat16)
    right_a = (scaled[:cut, :] * kept[:cut, None]).astype(jnp.bfloat16)
    left_a_got = shifted(left_a, "seg", 1)
    right_a_got = shifted(right_a, "seg", -1)
    left_in = env_update(left_mix, left_a_got)
    right_in = env_update(right_mix, right_a_got.T)
    ground, energy = lanczos(
        psi_one, left_in, right_in, mask, math.sqrt(blocks * width * width)
    )
    return (ground[None, None], jnp.reshape(energy, (1,)))


def solution(mesh):
    in_specs = (
        P("seg", "bond", None, None),
        P("seg", "bond", None, None, None),
        P("seg", "bond", None, None, None),
        P(),
        P("seg", "bond"),
        P("seg", "bond"),
    )
    out_specs = (P("seg", "bond", None, None), P("seg"))
    return jax.shard_map(
        per_device, mesh=mesh, in_specs=in_specs, out_specs=out_specs, check_vma=False
    )
```

```python
import functools
import math

import jax
import jax.numpy as jnp
from jax import lax
from jax.experimental import pallas as pl
from jax.experimental.pallas import tpu as pltpu
from jax.sharding import PartitionSpec as P

LANCZOS = 4
POWER = 4


def shifted(value, axis, steps):
    count = lax.axis_size(axis)
    pairs = [(source, (source + steps) % count) for source in range(count)]
    return lax.ppermute(value, axis, pairs)


def bond_sum(value, hooks=None):
    hooks = hooks or {}
    count = lax.axis_size("bond")
    if count & (count - 1):
        for index in sorted(hooks):
            value = hooks[index](value)
        return lax.psum(value, "bond")
    rounds = count.bit_length() - 1
    for index in range(rounds):
        if index in hooks:
            value = hooks[index](value)
        pairs = [(source, source ^ (1 << index)) for source in range(count)]
        value = value + lax.ppermute(value, "bond", pairs)
    for index in sorted(hooks):
        if index >= rounds:
            value = hooks[index](value)
    return value


def apply_ham(vector, left, right, mask):
    rounded = (vector * mask).astype(jnp.bfloat16)
    inner = jnp.einsum("ij,wjk->wik", rounded, right, preferred_element_type=jnp.float32).astype(
        jnp.bfloat16
    )
    outer = jnp.einsum("wij,wjk->ik", left, inner, preferred_element_type=jnp.float32)
    return outer * mask


def gram_kernel(head_ref, *refs):
    *vec_refs, out_ref = refs
    size = len(vec_refs)
    row = lax.broadcasted_iota(jnp.int32, out_ref.shape, 0)
    lane = lax.broadcasted_iota(jnp.int32, out_ref.shape, 1)
    out = jnp.zeros(out_ref.shape, jnp.float32)
    slot = 0
    for i in range(size):
        for j in range(i, size):
            if i == 0 and j == 0:
                head = head_ref[...]
                total = jnp.sum(head * head, axis=(0, 1), keepdims=True)
            else:
                total = jnp.sum(vec_refs[i][...] * vec_refs[j][...], axis=(0, 1), keepdims=True)
            out = jnp.where((row == 0) & (lane == slot), total, out)
            slot += 1
    out_ref[...] = out


def ritz_coefficients(total_ref, shape):
    size = LANCZOS + 1
    slots = {}
    slot = 0
    for i in range(size):
        for j in range(i, size):
            slots[i, j] = slots[j, i] = slot
            slot += 1
    entries = {}
    for key in range(slot):
        entries[key] = jnp.full(shape, total_ref[0, key], jnp.float32)
    gram = [[entries[slots[i, j]] for j in range(size)] for i in range(size)]
    zero = jnp.zeros(shape, jnp.float32)

    def quad(first, second):
        acc = zero
        for i in range(size):
            for j in range(size):
                acc = acc + first[i] * gram[i][j] * second[j]
        return acc

    def combine(first, scale_first, second, scale_second):
        return [a * scale_first + b * scale_second for a, b in zip(first, second)]

    vector = [1.0 / jnp.sqrt(gram[0][0])] + [zero] * (size - 1)
    previous = [zero] * size
    beta_prev = zero
    alphas = []
    betas = []
    basis = []
    for step in range(LANCZOS):
        image = [zero] + vector[:-1]
        alpha = quad(image, vector)
        image = [w - alpha * v - beta_prev * p for w, v, p in zip(image, vector, previous)]
        alphas.append(alpha)
        basis.append(vector)
        if step + 1 < LANCZOS:
            beta = jnp.sqrt(quad(image, image))
            betas.append(beta)
            previous = vector
            vector = [w / beta for w in image]
            beta_prev = beta

    def tri_times(weights):
        rows = []
        for i in range(LANCZOS):
            acc = alphas[i] * weights[i]
            if i > 0:
                acc = acc + betas[i - 1] * weights[i - 1]
            if i + 1 < LANCZOS:
                acc = acc + betas[i] * weights[i + 1]
            rows.append(acc)
        return rows

    sigma = None
    for i in range(LANCZOS):
        bound = alphas[i]
        if i > 0:
            bound = bound + jnp.abs(betas[i - 1])
        if i + 1 < LANCZOS:
            bound = bound + jnp.abs(betas[i])
        sigma = bound if sigma is None else jnp.maximum(sigma, bound)
    weights = [zero + 1.0] + [zero] * (LANCZOS - 1)
    for turn in range(POWER):
        product = tri_times(weights)
        weights = [sigma * w - t for w, t in zip(weights, product)]
        norm = zero
        for w in weights:
            norm = norm + w * w
        norm = jnp.sqrt(norm)
        weights = [w / norm for w in weights]
    product = tri_times(weights)
    energy = zero
    for w, t in zip(weights, product):
        energy = energy + w * t
    coef = [c * weights[0] for c in basis[0]]
    for step in range(1, LANCZOS):
        coef = [c + weights[step] * b for c, b in zip(coef, basis[step])]
    return coef, energy


def finish_kernel(total_ref, head_ref, *refs, scale, cut, rank_scale):
    if rank_scale is None:
        *vec_refs, out_ref, energy_ref = refs
    else:
        rank_ref, *vec_refs, out_ref, left_ref, right_ref = refs
    coef, energy = ritz_coefficients(total_ref, (8, 128))
    coef = [c[:1, :1] for c in coef]
    rows, cols = vec_refs[0].shape
    acc = vec_refs[0][...] * coef[0]
    for step in range(1, len(vec_refs)):
        acc = acc + coef[step] * vec_refs[step][...]
    if scale is not None:
        acc = acc * scale
    if head_ref.shape != vec_refs[0].shape:
        rest = head_ref[...] * coef[0]
        if scale is not None:
            rest = rest * scale
        out_ref[...] = rest
    out_ref[:rows, :cols] = acc
    if rank_scale is None:
        energy_ref[...] = energy[:1, :1]
    else:
        rank = rank_ref[0, 0]
        scaled = out_ref[...] * rank_scale
        width = scaled.shape[0]
        col = lax.broadcasted_iota(jnp.int32, (width, cut), 1)
        left_ref[...] = (scaled[:, :cut] * (col < rank).astype(jnp.float32)).astype(jnp.bfloat16)
        row = lax.broadcasted_iota(jnp.int32, (cut, width), 0)
        right_ref[...] = (scaled[:cut, :] * (row < rank).astype(jnp.float32)).astype(jnp.bfloat16)


def lanczos(start, left, right, mask, scale=None, cut=None, hooks=None, rank=None):
    head = start * mask
    if cut is None:
        base, live = head, mask
    else:
        base, live = head[:cut, :cut], mask[:cut, :cut]
    krylov = [base]
    for step in range(LANCZOS):
        krylov.append(apply_ham(krylov[-1], left, right, live))
    tile = jax.ShapeDtypeStruct((8, 128), jnp.float32)
    local = pl.pallas_call(gram_kernel, out_shape=tile)(head, *krylov)
    total = bond_sum(local, hooks)
    smem = pl.BlockSpec(memory_space=pltpu.SMEM)
    vmem = pl.BlockSpec(memory_space=pltpu.VMEM)
    width = head.shape[-1]
    field = jax.ShapeDtypeStruct(head.shape, jnp.float32)
    if rank is None:
        in_specs = [smem, vmem] + [vmem] * LANCZOS
        out_shape = (field, jax.ShapeDtypeStruct((1, 1), jnp.float32))
        extra = ()
        rank_scale = None
    else:
        in_specs = [smem, vmem, smem] + [vmem] * LANCZOS
        out_shape = (
            field,
            jax.ShapeDtypeStruct((width, width // 2), jnp.bfloat16),
            jax.ShapeDtypeStruct((width // 2, width), jnp.bfloat16),
        )
        extra = (rank,)
        rank_scale = math.sqrt(lax.axis_size("bond") * width)
    return pl.pallas_call(
        functools.partial(
            finish_kernel, scale=scale, cut=width // 2, rank_scale=rank_scale
        ),
        out_shape=out_shape,
        in_specs=in_specs,
    )(total, head, *extra, *krylov[:LANCZOS])


def env_update(mixed, left_a):
    half_left = jnp.einsum(
        "wij,jk->wik", mixed, left_a, preferred_element_type=jnp.float32
    ).astype(jnp.bfloat16)
    return jnp.einsum(
        "ji,wjk->wik", left_a, half_left, preferred_element_type=jnp.float32
    ).astype(jnp.bfloat16)


def per_device(state, left_env, right_env, mpo_mix, block_sizes, ranks):
    blocks = lax.axis_size("bond")
    width = state.shape[-1]
    start = state[0, 0]
    left = left_env[0, 0]
    right = right_env[0, 0]
    index = jnp.arange(width, dtype=jnp.int32)
    live = (index < block_sizes[0, 0]).astype(jnp.float32)
    mask = live[:, None] * live[None, :]
    kept = (index < ranks[0, 0]).astype(jnp.float32)
    left_got = shifted(left, "seg", 1)
    right_got = shifted(right, "seg", -1)

    def mixed(env):
        return jnp.einsum(
            "wu,uij->wij", mpo_mix, env.astype(jnp.float32), precision=lax.Precision.HIGHEST
        ).astype(jnp.bfloat16)

    held = {}

    def take_envs(value):
        value, held["left"], held["right"] = lax.optimization_barrier((value, left_got, right_got))
        return value

    def mix_left(value):
        value, held["left"] = lax.optimization_barrier((value, mixed(held["left"])))
        return value

    def mix_right(value):
        value, held["right"] = lax.optimization_barrier((value, mixed(held["right"])))
        return value

    hooks = {1: take_envs, 3: mix_left, 4: mix_right}
    cut = width // 2
    psi_one, left_a, right_a = lanczos(start, left, right, mask, hooks=hooks, rank=ranks)
    left_mix, right_mix = held["left"], held["right"]
    left_a_got = shifted(left_a, "seg", 1)
    right_a_got = shifted(right_a, "seg", -1)
    left_in = env_update(left_mix, left_a_got)
    right_in = env_update(right_mix, right_a_got.T)
    ground, energy = lanczos(
        psi_one, left_in, right_in, mask, math.sqrt(blocks * width * width), cut
    )
    return (ground[None, None], jnp.reshape(energy, (1,)))


def solution(mesh):
    in_specs = (
        P("seg", "bond", None, None),
        P("seg", "bond", None, None, None),
        P("seg", "bond", None, None, None),
        P(),
        P("seg", "bond"),
        P("seg", "bond"),
    )
    out_specs = (P("seg", "bond", None, None), P("seg"))
    return jax.shard_map(
        per_device, mesh=mesh, in_specs=in_specs, out_specs=out_specs, check_vma=False
    )
```

```python
import functools
import math

import jax
import jax.numpy as jnp
from jax import lax
from jax.experimental import pallas as pl
from jax.experimental.pallas import tpu as pltpu
from jax.sharding import PartitionSpec as P

LANCZOS = 4
POWER = 4


def shifted(value, axis, steps):
    count = lax.axis_size(axis)
    pairs = [(source, (source + steps) % count) for source in range(count)]
    return lax.ppermute(value, axis, pairs)


def bond_sum(value, hooks=None):
    hooks = hooks or {}
    count = lax.axis_size("bond")
    if count & (count - 1):
        for index in sorted(hooks):
            value = hooks[index](value)
        return lax.psum(value, "bond")
    rounds = count.bit_length() - 1
    for index in range(rounds):
        if index in hooks:
            value = hooks[index](value)
        pairs = [(source, source ^ (1 << index)) for source in range(count)]
        value = value + lax.ppermute(value, "bond", pairs)
    for index in sorted(hooks):
        if index >= rounds:
            value = hooks[index](value)
    return value


def apply_ham(vector, left, right, mask):
    rounded = (vector * mask).astype(jnp.bfloat16)
    inner = jnp.einsum("ij,wjk->wik", rounded, right, preferred_element_type=jnp.float32).astype(
        jnp.bfloat16
    )
    outer = jnp.einsum("wij,wjk->ik", left, inner, preferred_element_type=jnp.float32)
    return outer * mask


def gram_kernel(start_ref, mask_ref, *refs):
    *later_refs, out_ref = refs
    head = start_ref[...] * mask_ref[...]
    n = later_refs[0].shape[-1]
    vecs = [lambda: head[:n, :n]] + [lambda ref=ref: ref[...] for ref in later_refs]
    size = len(vecs)
    row = lax.broadcasted_iota(jnp.int32, out_ref.shape, 0)
    lane = lax.broadcasted_iota(jnp.int32, out_ref.shape, 1)
    out = jnp.zeros(out_ref.shape, jnp.float32)
    slot = 0
    for i in range(size):
        for j in range(i, size):
            if i == 0 and j == 0:
                total = jnp.sum(head * head, axis=(0, 1), keepdims=True)
            else:
                total = jnp.sum(vecs[i]() * vecs[j](), axis=(0, 1), keepdims=True)
            out = jnp.where((row == 0) & (lane == slot), total, out)
            slot += 1
    out_ref[...] = out


def ritz_coefficients(total_ref, shape):
    size = LANCZOS + 1
    slots = {}
    slot = 0
    for i in range(size):
        for j in range(i, size):
            slots[i, j] = slots[j, i] = slot
            slot += 1
    entries = {}
    for key in range(slot):
        entries[key] = jnp.full(shape, total_ref[0, key], jnp.float32)
    gram = [[entries[slots[i, j]] for j in range(size)] for i in range(size)]
    zero = jnp.zeros(shape, jnp.float32)

    def quad(first, second):
        acc = zero
        for i in range(size):
            for j in range(size):
                acc = acc + first[i] * gram[i][j] * second[j]
        return acc

    def combine(first, scale_first, second, scale_second):
        return [a * scale_first + b * scale_second for a, b in zip(first, second)]

    vector = [1.0 / jnp.sqrt(gram[0][0])] + [zero] * (size - 1)
    previous = [zero] * size
    beta_prev = zero
    alphas = []
    betas = []
    basis = []
    for step in range(LANCZOS):
        image = [zero] + vector[:-1]
        alpha = quad(image, vector)
        image = [w - alpha * v - beta_prev * p for w, v, p in zip(image, vector, previous)]
        alphas.append(alpha)
        basis.append(vector)
        if step + 1 < LANCZOS:
            beta = jnp.sqrt(quad(image, image))
            betas.append(beta)
            previous = vector
            vector = [w / beta for w in image]
            beta_prev = beta

    def tri_times(weights):
        rows = []
        for i in range(LANCZOS):
            acc = alphas[i] * weights[i]
            if i > 0:
                acc = acc + betas[i - 1] * weights[i - 1]
            if i + 1 < LANCZOS:
                acc = acc + betas[i] * weights[i + 1]
            rows.append(acc)
        return rows

    sigma = None
    for i in range(LANCZOS):
        bound = alphas[i]
        if i > 0:
            bound = bound + jnp.abs(betas[i - 1])
        if i + 1 < LANCZOS:
            bound = bound + jnp.abs(betas[i])
        sigma = bound if sigma is None else jnp.maximum(sigma, bound)
    weights = [zero + 1.0] + [zero] * (LANCZOS - 1)
    for turn in range(POWER):
        product = tri_times(weights)
        weights = [sigma * w - t for w, t in zip(weights, product)]
        norm = zero
        for w in weights:
            norm = norm + w * w
        norm = jnp.sqrt(norm)
        weights = [w / norm for w in weights]
    product = tri_times(weights)
    energy = zero
    for w, t in zip(weights, product):
        energy = energy + w * t
    coef = [c * weights[0] for c in basis[0]]
    for step in range(1, LANCZOS):
        coef = [c + weights[step] * b for c, b in zip(coef, basis[step])]
    return coef, energy


def finish_kernel(total_ref, start_ref, mask_ref, *refs, scale, cut, rank_scale):
    if rank_scale is None:
        *later_refs, out_ref, energy_ref = refs
    else:
        rank_ref, *later_refs, out_ref, left_ref, right_ref = refs
    coef, energy = ritz_coefficients(total_ref, (8, 128))
    coef = [c[:1, :1] for c in coef]
    head = start_ref[...] * mask_ref[...]
    rows, cols = later_refs[0].shape
    acc = head[:rows, :cols] * coef[0]
    for step in range(1, LANCZOS):
        acc = acc + coef[step] * later_refs[step - 1][...]
    if scale is not None:
        acc = acc * scale
    if head.shape != (rows, cols):
        rest = head * coef[0]
        if scale is not None:
            rest = rest * scale
        out_ref[...] = rest
    out_ref[:rows, :cols] = acc
    if rank_scale is None:
        energy_ref[...] = energy[:1, :1]
    else:
        rank = rank_ref[0, 0]
        scaled = out_ref[...] * rank_scale
        width = scaled.shape[0]
        col = lax.broadcasted_iota(jnp.int32, (width, cut), 1)
        left_ref[...] = (scaled[:, :cut] * (col < rank).astype(jnp.float32)).astype(jnp.bfloat16)
        row = lax.broadcasted_iota(jnp.int32, (cut, width), 0)
        right_ref[...] = (scaled[:cut, :] * (row < rank).astype(jnp.float32)).astype(jnp.bfloat16)


def lanczos(start, left, right, mask, scale=None, cut=None, hooks=None, rank=None):
    head = start * mask
    if cut is None:
        base, live = head, mask
    else:
        base, live = head[:cut, :cut], mask[:cut, :cut]
    krylov = [base]
    for step in range(LANCZOS):
        krylov.append(apply_ham(krylov[-1], left, right, live))
    tile = jax.ShapeDtypeStruct((8, 128), jnp.float32)
    local = pl.pallas_call(gram_kernel, out_shape=tile)(start, mask, *krylov[1:])
    total = bond_sum(local, hooks)
    smem = pl.BlockSpec(memory_space=pltpu.SMEM)
    vmem = pl.BlockSpec(memory_space=pltpu.VMEM)
    width = head.shape[-1]
    field = jax.ShapeDtypeStruct(head.shape, jnp.float32)
    if rank is None:
        in_specs = [smem, vmem, vmem] + [vmem] * (LANCZOS - 1)
        out_shape = (field, jax.ShapeDtypeStruct((1, 1), jnp.float32))
        extra = ()
        rank_scale = None
    else:
        in_specs = [smem, vmem, vmem, smem] + [vmem] * (LANCZOS - 1)
        out_shape = (
            field,
            jax.ShapeDtypeStruct((width, width // 2), jnp.bfloat16),
            jax.ShapeDtypeStruct((width // 2, width), jnp.bfloat16),
        )
        extra = (rank,)
        rank_scale = math.sqrt(lax.axis_size("bond") * width)
    return pl.pallas_call(
        functools.partial(
            finish_kernel, scale=scale, cut=width // 2, rank_scale=rank_scale
        ),
        out_shape=out_shape,
        in_specs=in_specs,
    )(total, start, mask, *extra, *krylov[1:LANCZOS])


def env_update(mixed, left_a):
    half_left = jnp.einsum(
        "wij,jk->wik", mixed, left_a, preferred_element_type=jnp.float32
    ).astype(jnp.bfloat16)
    return jnp.einsum(
        "ji,wjk->wik", left_a, half_left, preferred_element_type=jnp.float32
    ).astype(jnp.bfloat16)


def per_device(state, left_env, right_env, mpo_mix, block_sizes, ranks):
    blocks = lax.axis_size("bond")
    width = state.shape[-1]
    start = state[0, 0]
    left = left_env[0, 0]
    right = right_env[0, 0]
    index = jnp.arange(width, dtype=jnp.int32)
    live = (index < block_sizes[0, 0]).astype(jnp.float32)
    mask = live[:, None] * live[None, :]
    kept = (index < ranks[0, 0]).astype(jnp.float32)
    left_got = shifted(left, "seg", 1)
    right_got = shifted(right, "seg", -1)

    def mixed(env):
        return jnp.einsum(
            "wu,uij->wij", mpo_mix, env.astype(jnp.float32), precision=lax.Precision.HIGHEST
        ).astype(jnp.bfloat16)

    held = {}

    def take_envs(value):
        value, held["left"], held["right"] = lax.optimization_barrier((value, left_got, right_got))
        return value

    def mix_left(value):
        value, held["left"] = lax.optimization_barrier((value, mixed(held["left"])))
        return value

    def mix_right(value):
        value, held["right"] = lax.optimization_barrier((value, mixed(held["right"])))
        return value

    hooks = {1: take_envs, 3: mix_left, 4: mix_right}
    cut = width // 2
    psi_one, left_a, right_a = lanczos(start, left, right, mask, hooks=hooks, rank=ranks)
    left_mix, right_mix = held["left"], held["right"]
    left_a_got = shifted(left_a, "seg", 1)
    right_a_got = shifted(right_a, "seg", -1)
    left_in = env_update(left_mix, left_a_got)
    right_in = env_update(right_mix, right_a_got.T)
    ground, energy = lanczos(
        psi_one, left_in, right_in, mask, math.sqrt(blocks * width * width), cut
    )
    return (ground[None, None], jnp.reshape(energy, (1,)))


def solution(mesh):
    in_specs = (
        P("seg", "bond", None, None),
        P("seg", "bond", None, None, None),
        P("seg", "bond", None, None, None),
        P(),
        P("seg", "bond"),
        P("seg", "bond"),
    )
    out_specs = (P("seg", "bond", None, None), P("seg"))
    return jax.shard_map(
        per_device, mesh=mesh, in_specs=in_specs, out_specs=out_specs, check_vma=False
    )
```
